256 devices in a mesh: seq: 32 (over z, y), tp: 8 (over x, core).
Axes of the slice: x: 4, y: 4, z: 8, core: 2. Of those that a mesh axis runs over, the one named last changes fastest.
Arguments:
- embedded: bfloat16 [32, 4, 1536], replicated, may hold values from -45 to 45
- lengths: int32 [32], replicated, may hold values from 1 to 32768, 524288 in all
- routes: int32 [128, 8], replicated, may hold values from 0 to 39, all different within a row; in each aligned block of 128 rows (0 to 127, 128 to 255, ...) at most 64 rows name the same one
- attn_gain: float32 [1536], replicated, may hold values from 0.1 to 1.9
- query_key_value_weight: bfloat16 [1536, 8, 320], P(None, 'tp'), may hold values from -0.15625 to 0.15625
- cache_k: bfloat16 [32, 8, 32768, 64], P(None, 'tp', 'seq'), may hold values from -350 to 350
- value_cache: bfloat16 [32, 8, 32768, 64], P(None, 'tp', 'seq'), may hold values from -6 to 6
- output_weight: bfloat16 [8, 192, 1536], P('tp'), may hold values from -0.75 to 0.75
- moe_gain: float32 [1536], replicated, may hold values from 0.1 to 1.9
- w_router: bfloat16 [1536, 40], P('seq'), may hold values from -13 to 13
- w_gate_up: bfloat16 [40, 1536, 2, 512], P('tp', 'seq'), may hold values from -0.15625 to 0.15625
- w_down: bfloat16 [40, 1536, 512], P('tp', 'seq'), may hold values from -0.25 to 0.25
Outputs:
- result: bfloat16 [128, 1536], P('tp', 'seq')
The draws below stay inside these ranges and needn't reach their ends.
Inputs may be any that keep to these rules, and one draw needn't show every extreme that they name: `lengths`: the positions below a request's length hold its earlier keys and values; the longest request fills all 32768 positions. `routes`: each token names 8 distinct experts; over all 128 tokens no expert is named more than 64 times, a bound that some block reaches.
All inputs are finite; a program needn't handle non-finite values.
Results may differ from the reference program's by a relative error of at most 0.035.
Values may be sent and summed in bfloat16 or wider, within the bound.
No kernel may reach another device: no remote copies, remote signals or barrier semaphores. Data moves between devices by JAX's collectives and lax.ppermute only.
A program may use at most 64 MiB of HBM per device.

```python
import math
import jax
import jax.numpy as jnp
import numpy as np
from jax import lax

MODEL_WIDTH = 1536
KEY_VALUE_HEADS = 8
HEAD_WIDTH = 64
EXPERTS = 40
HID = 512
TOP = 8
QUERIES_PER_KEY = 3
FRESH_TOKENS = 4
REQUEST_COUNT = 32
CACHE_POSITIONS = 32768
TOKEN_TOTAL = 128
CAP = 64


def draw_embedded(key, part):
    first = jax.random.fold_in(key, 0)
    ramp = 0.5 + jnp.arange(MODEL_WIDTH, dtype=jnp.float32) / MODEL_WIDTH
    return (jnp.clip(jax.random.normal(first, (REQUEST_COUNT, FRESH_TOKENS, MODEL_WIDTH), jnp.float32), -6.0, 6.0) * ramp).astype(jnp.bfloat16)


def draw_cache_k(key, part):
    first = jax.random.fold_in(key, 0)
    array_shape = (REQUEST_COUNT, KEY_VALUE_HEADS, CACHE_POSITIONS, HEAD_WIDTH)
    return jnp.clip(jax.random.normal(first, array_shape, jnp.float32), -6.0, 6.0).astype(jnp.bfloat16)


def draw_w_router(key, part):
    scale = 1.0 / math.sqrt(MODEL_WIDTH)
    return (jnp.clip(jax.random.normal(key, (MODEL_WIDTH, EXPERTS), jnp.float32), -6.0, 6.0) * scale).astype(jnp.bfloat16)


def block_scale(key, dims, cuts, low, high):
    factor_of, own = 1.0, jax.random.fold_in(key, 6)
    for axis_at, parts in cuts:
        heights = jnp.exp(jax.random.uniform(jax.random.fold_in(own, axis_at), (parts,), jnp.float32, low / len(cuts), high / len(cuts)))
        factor_of = factor_of * jnp.repeat(heights, dims[axis_at] // parts).reshape([-1 if axis == axis_at else 1 for axis in range(len(dims))])
    return factor_of


def length_profile(count, total, most, slope):
    loads = [(1 << 20) // math.isqrt(rank ** slope) + 1 for rank in range(2, count + 1)]
    surplus, holding = total - most - (count - 1), [1] * (count - 1)
    while surplus > 0:
        movable = [i for i in range(count - 1) if holding[i] < most]
        pool, left = sum([loads[i] for i in movable]), surplus
        for i in movable:
            more = min(most - holding[i], max(1, left * loads[i] // pool), surplus)
            holding[i] = holding[i] + more
            surplus = surplus - more
    return np.array([most] + holding)


def ragged(key, amount, total, reach, skew):
    if amount == 2:
        one = jax.random.randint(key, (), max(1, total - reach), min(reach, total - 1) + 1)
        return jnp.stack([one, total - one])
    sizes = jnp.asarray(length_profile(amount, total, reach, skew), jnp.int32)
    couples = (amount - 1) // 2
    source_of, sink = sizes[1:1 + 2 * couples:2], sizes[2:2 + 2 * couples:2]
    room = jnp.minimum(source_of - 1, reach - sink)
    passed = jax.random.randint(jax.random.fold_in(key, 1), (couples,), 0, 1 << 20) % (room + 1)
    sizes = sizes.at[1:1 + 2 * couples:2].set(source_of - passed).at[2:2 + 2 * couples:2].set(sink + passed)
    return sizes[jax.random.permutation(jax.random.fold_in(key, 2), amount)]


def shared_out(key, own, number, rows, amount, top, limit, skew):
    order = jax.random.permutation(key, amount)
    heavy_load, usual = load_shares(amount, rows * top, limit, skew, True), load_shares(amount, rows * top, limit, skew, False)
    places = jnp.arange(amount)

    def named(sizes, offset_by):
        used = int((sizes > 0).sum())
        fixed = max(1, used // 4)
        passed = fixed + (places - fixed + offset_by * (used - fixed)) % max(1, amount - fixed)
        return jnp.zeros((amount,), jnp.int32).at[order[jnp.where(places < fixed, places, passed)]].set(jnp.asarray(sizes, jnp.int32))

    sizes = jnp.where(number % 4 == 0, named(heavy_load, number // 4), named(usual, number - number // 4 - 1))
    mixed = jax.random.permutation(jax.random.fold_in(own, 3), amount)
    donor, sink = mixed[0:amount // 2 * 2:2], mixed[1:amount // 2 * 2:2]
    margin = jnp.minimum(sizes[donor] - 1, limit - sizes[sink]) // 2
    margin = jnp.where((donor == order[0]) | (sink == order[0]) | (sizes[sink] == 0), 0, jnp.maximum(margin, 0))
    passed = jax.random.randint(jax.random.fold_in(own, 4), (amount // 2,), 0, 1 << 20) % (margin + 1)
    sizes = sizes.at[donor].add(-passed).at[sink].add(passed)
    items = jnp.searchsorted(jnp.cumsum(sizes), jnp.arange(rows * top), side="right").astype(jnp.int32)
    table = items.reshape(top, rows).T
    table = table[jax.random.permutation(jax.random.fold_in(own, 1), rows)]
    offset_by = jax.random.randint(jax.random.fold_in(own, 2), (rows, 1), 0, top)
    return jnp.take_along_axis(table, (jnp.arange(top)[None, :] + offset_by) % top, axis=1)


def load_shares(number_of, total, bound, skew, full):
    loads = [(1 << 20) // math.isqrt(grade ** skew) + 1 for grade in range(1, number_of + 1)]
    largest = bound if full else min(bound, max(-(-total // number_of), total * loads[0] // sum(loads)))
    least = 1 if total - largest >= number_of - 1 else 0
    holding, spare = [largest] + [least] * (number_of - 1), total - largest - least * (number_of - 1)
    while spare > 0:
        candidates = [i for i in range(1, number_of) if holding[i] < largest] or [i for i in range(1, number_of) if holding[i] < bound]
        pool, budget = sum([loads[i] for i in candidates]), spare
        for i in candidates:
            extra = min(bound - holding[i], max(1, budget * loads[i] // pool), spare)
            holding[i] = holding[i] + extra
            spare = spare - extra
    return np.array(holding)


def noise(stream_key, extent, width, limit, pieces=(), held_as=jnp.bfloat16):
    entries = jax.random.normal(stream_key, extent, jnp.float32) * width
    if len(pieces) > 0:
        entries = block_scale(stream_key, extent, pieces, -0.22, 0.18) * entries
    return jnp.clip(entries, min=-limit, max=limit).astype(held_as)


def setup_inputs(seed: int = 0) -> dict:
    splits = jax.random.split(jax.random.key(seed), 13)
    embedded = draw_embedded(jax.random.fold_in(splits[12], 71), 0)
    lengths = ragged(splits[1], REQUEST_COUNT, REQUEST_COUNT * CACHE_POSITIONS // 2, CACHE_POSITIONS, 2).astype(jnp.int32)
    routes_keys = jax.random.split(jax.random.fold_in(splits[2], 1), TOKEN_TOTAL // TOKEN_TOTAL)
    routes_turns = jax.random.permutation(jax.random.fold_in(splits[2], 3), TOKEN_TOTAL // TOKEN_TOTAL)
    routes = jax.vmap(lambda own, number: shared_out(jax.random.fold_in(splits[2], 2), own, number, TOKEN_TOTAL, EXPERTS, TOP, CAP, 2))(routes_keys, routes_turns).reshape((TOKEN_TOTAL, TOP))
    attn_gain = jnp.clip(1.0 + 0.18 * jax.random.normal(splits[3], (MODEL_WIDTH,), jnp.float32), 0.1, 1.9)
    query_key_value_weight = noise(splits[4], (MODEL_WIDTH, KEY_VALUE_HEADS, (QUERIES_PER_KEY + 2) * HEAD_WIDTH), MODEL_WIDTH ** -0.5, 0.15625, ((1, 8),))
    cache_k = draw_cache_k(jax.random.fold_in(splits[12], 71), 0)
    value_cache = noise(splits[6], (REQUEST_COUNT, KEY_VALUE_HEADS, CACHE_POSITIONS, HEAD_WIDTH), 1.0, 6.0, ((1, 8), (2, 32)))
    output_weight = noise(splits[7], (KEY_VALUE_HEADS, QUERIES_PER_KEY * HEAD_WIDTH, MODEL_WIDTH), HEAD_WIDTH ** -0.5, 0.75, ((0, 8),))
    moe_gain = jnp.clip(1.0 + 0.18 * jax.random.normal(splits[8], (MODEL_WIDTH,), jnp.float32), 0.1, 1.9)
    w_router = draw_w_router(jax.random.fold_in(splits[12], 71), 0)
    w_gate_up = noise(splits[10], (EXPERTS, MODEL_WIDTH, 2, HID), MODEL_WIDTH ** -0.5, 0.15625, ((0, 8), (1, 32)))
    w_down = noise(splits[11], (EXPERTS, MODEL_WIDTH, HID), HID ** -0.5, 0.25, ((0, 8), (1, 32)))
    return dict(embedded=embedded, lengths=lengths, routes=routes, attn_gain=attn_gain, query_key_value_weight=query_key_value_weight, cache_k=cache_k, value_cache=value_cache, output_weight=output_weight, moe_gain=moe_gain, w_router=w_router, w_gate_up=w_gate_up, w_down=w_down)


EPSILON = 1e-06
ROPE_BASE = 10000.0
SCORE_SCALE = 0.125
NEG_LARGE = -1e+30

def rms_scale(values, gain):
    stat = lax.optimization_barrier(jnp.mean(values * values, axis=-1, keepdims=True))
    return values * lax.rsqrt(stat + EPSILON) * gain

def rotate(values, angles):
    half = values.shape[-1] // 2
    cosine = jnp.cos(angles)
    sine = jnp.sin(angles)
    front = values[..., :half]
    back = values[..., half:]
    return jnp.concatenate([front * cosine - back * sine, back * cosine + front * sine], axis=-1)

def reference(embedded, lengths, routes, attn_gain, query_key_value_weight, cache_k, value_cache, output_weight, moe_gain, w_router, w_gate_up, w_down):
    head_extent = cache_k.shape[3]
    head_groups = query_key_value_weight.shape[2] // head_extent - 2
    inputs = embedded.astype(jnp.float32)
    normed = rms_scale(inputs, attn_gain).astype(jnp.bfloat16)
    projected_rows = jnp.einsum('rtd,dhc->rthc', normed.astype(jnp.float32), query_key_value_weight.astype(jnp.float32))
    split_parts = projected_rows.reshape(REQUEST_COUNT, FRESH_TOKENS, KEY_VALUE_HEADS, head_groups + 2, head_extent)
    half = head_extent // 2
    freqs = ROPE_BASE ** (-jnp.arange(half, dtype=jnp.float32) / half)
    positions = lengths.astype(jnp.float32)[:, None] + jnp.arange(FRESH_TOKENS, dtype=jnp.float32)[None, :]
    angles = positions[:, :, None] * freqs
    queries = rotate(split_parts[:, :, :, :head_groups], angles[:, :, None, None, :]).astype(jnp.bfloat16)
    new_keys = rotate(split_parts[:, :, :, head_groups], angles[:, :, None, :]).astype(jnp.bfloat16)
    new_values = split_parts[:, :, :, head_groups + 1].astype(jnp.bfloat16)

    def attend(item):
        query_rows, key_rows, value_rows, old_keys, old_values, length = item
        all_keys = jnp.concatenate([old_keys, jnp.swapaxes(key_rows, 0, 1)], axis=1).astype(jnp.float32)
        all_values = jnp.concatenate([old_values, jnp.swapaxes(value_rows, 0, 1)], axis=1).astype(jnp.float32)
        scores = jnp.einsum('thqe,hpe->hqtp', query_rows.astype(jnp.float32), all_keys) * SCORE_SCALE
        places = jnp.arange(CACHE_POSITIONS + FRESH_TOKENS, dtype=jnp.int32)
        newest = jnp.arange(FRESH_TOKENS, dtype=jnp.int32)
        allowed = jnp.where(places[None, :] < CACHE_POSITIONS, places[None, :] < length, places[None, :] - CACHE_POSITIONS <= newest[:, None])
        masked = jnp.where(allowed, scores, NEG_LARGE)
        highest = lax.optimization_barrier(jnp.max(masked, axis=-1, keepdims=True))
        probs = jnp.where(allowed, jnp.exp(masked - highest), 0.0)
        totals = lax.optimization_barrier(jnp.sum(probs, axis=-1, keepdims=True))
        rounded = lax.optimization_barrier(probs.astype(jnp.bfloat16)).astype(jnp.float32)
        summed = jnp.einsum('hqtp,hpe->thqe', rounded, all_values)
        return (summed / jnp.transpose(totals, (2, 0, 1, 3))).astype(jnp.bfloat16)
    attention_result = lax.map(attend, (queries, new_keys, new_values, cache_k, value_cache, lengths))
    flattened_rows = lax.optimization_barrier(attention_result).reshape(TOKEN_TOTAL, KEY_VALUE_HEADS, head_groups * head_extent).astype(jnp.float32)
    residual = inputs.reshape(TOKEN_TOTAL, MODEL_WIDTH) + jnp.einsum('nhc,hcd->nd', flattened_rows, output_weight.astype(jnp.float32))
    mixed_rows = rms_scale(residual, moe_gain).astype(jnp.bfloat16)
    logits = jnp.dot(mixed_rows, w_router, preferred_element_type=jnp.float32)
    choose = routes[:, :, None] == jnp.arange(EXPERTS, dtype=jnp.int32)[None, None, :]
    picked = lax.optimization_barrier(jnp.sum(jnp.where(choose, logits[:, None, :], 0.0), axis=-1))
    combine = jax.nn.softmax(picked, axis=-1)
    flat_routes = routes.reshape(-1)
    onehot = (flat_routes[:, None] == jnp.arange(EXPERTS, dtype=jnp.int32)[None, :]).astype(jnp.int32)
    before = jnp.cumsum(onehot, axis=0) - onehot
    slots = lax.optimization_barrier(jnp.sum(before * onehot, axis=1)).reshape(TOKEN_TOTAL, TOP)
    slot_ids = jnp.arange(CAP, dtype=jnp.int32)
    mixed_float = mixed_rows.astype(jnp.float32)

    def run_expert(carry, expert):
        hits = (routes[None] == expert) & (slots[None] == slot_ids[:, None, None])
        dispatch = jnp.any(hits, axis=-1).astype(jnp.float32)
        slot_weight = lax.optimization_barrier(jnp.sum(jnp.where(hits, combine[None], 0.0), axis=(1, 2)))
        expert_in = jnp.dot(dispatch, mixed_float, precision=lax.Precision.HIGHEST)
        both = jnp.einsum('cd,dgh->cgh', expert_in, w_gate_up[expert].astype(jnp.float32))
        hidden = (jax.nn.silu(both[:, 0]) * both[:, 1] * slot_weight[:, None]).astype(jnp.bfloat16)
        hidden_float = lax.optimization_barrier(hidden).astype(jnp.float32)
        outputs = jnp.einsum('ch,dh->cd', hidden_float, w_down[expert].astype(jnp.float32))
        back = jnp.dot(dispatch.T, outputs, precision=lax.Precision.HIGHEST)
        return (carry + back, None)
    moe_total, unused = lax.scan(run_expert, jnp.zeros((TOKEN_TOTAL, MODEL_WIDTH), jnp.float32), jnp.arange(EXPERTS, dtype=jnp.int32))
    return (residual + moe_total).astype(jnp.bfloat16)
```

```python
import jax
import jax.numpy as jnp
from jax import lax
from jax.sharding import PartitionSpec as P

EPSILON = 1e-06
ROPE_BASE = 10000.0
SCORE_SCALE = 0.125
NEG_LARGE = -1e30


def rotate(values, angles):
    half = values.shape[-1] // 2
    cosine = jnp.cos(angles)
    sine = jnp.sin(angles)
    front = values[..., :half]
    back = values[..., half:]
    return jnp.concatenate([front * cosine - back * sine, back * cosine + front * sine], axis=-1)


def butterfly_sum(values, axis):
    count = lax.axis_size(axis)
    step = 1
    while step < count:
        pairs = [(i, i ^ step) for i in range(count)]
        values = values + lax.ppermute(values, axis, pairs)
        step *= 2
    return values


def per_device(
    embedded,
    lengths,
    routes,
    attn_gain,
    query_key_value_weight,
    cache_k,
    value_cache,
    output_weight,
    moe_gain,
    w_router,
    w_gate_up,
    w_down,
):
    requests, new_count, width = embedded.shape
    token_count = requests * new_count
    head_extent = cache_k.shape[3]
    head_groups = query_key_value_weight.shape[2] // head_extent - 2
    ctx_here = cache_k.shape[2]
    part_width = w_router.shape[0]
    seq_size = lax.axis_size("seq")
    tp_size = lax.axis_size("tp")
    seq_index = lax.axis_index("seq")
    tp_index = lax.axis_index("tp")
    own_request = seq_index * (requests // seq_size)

    inputs = embedded.astype(jnp.float32)
    stat = jnp.mean(inputs * inputs, axis=-1, keepdims=True)
    normed = (inputs * lax.rsqrt(stat + EPSILON) * attn_gain).astype(jnp.bfloat16)
    projected_rows = jnp.einsum(
        "rtd,dhc->rthc", normed, query_key_value_weight, preferred_element_type=jnp.float32
    )
    split_parts = projected_rows.reshape(requests, new_count, 1, head_groups + 2, head_extent)
    half = head_extent // 2
    freqs = ROPE_BASE ** (-jnp.arange(half, dtype=jnp.float32) / half)
    positions = (
        lengths.astype(jnp.float32)[:, None] + jnp.arange(new_count, dtype=jnp.float32)[None, :]
    )
    angles = positions[:, :, None] * freqs
    queries = rotate(split_parts[:, :, :, :head_groups], angles[:, :, None, None, :]).astype(
        jnp.bfloat16
    )
    new_keys = rotate(split_parts[:, :, :, head_groups], angles[:, :, None, :]).astype(jnp.bfloat16)
    new_values = split_parts[:, :, :, head_groups + 1].astype(jnp.bfloat16)

    with jax.named_scope("cache_attention"):
        scores = (
            jnp.einsum("rthqe,rhpe->rhqtp", queries, cache_k, preferred_element_type=jnp.float32)
            * SCORE_SCALE
        )
        places = seq_index * ctx_here + jnp.arange(ctx_here, dtype=jnp.int32)
        live = (places[None, :] < lengths[:, None])[:, None, None, None, :]
        masked = jnp.where(live, scores, NEG_LARGE)
        local_top = jnp.max(masked, axis=-1)
        probs = jnp.where(live, jnp.exp(masked - local_top[..., None]), 0.0)
        totals = jnp.sum(probs, axis=-1)
        sums = jnp.einsum(
            "rhqtp,rhpe->rhqte",
            probs.astype(jnp.bfloat16),
            value_cache,
            preferred_element_type=jnp.float32,
        )
    partial = jnp.concatenate([sums, totals[..., None], local_top[..., None]], axis=-1)
    partial = partial.reshape(seq_size, -1)
    router_rows = jnp.broadcast_to(
        w_router.astype(jnp.float32).reshape(1, -1), (seq_size, w_router.size)
    )
    with jax.named_scope("gather_partials"):
        received = lax.all_to_all(
            jnp.concatenate([partial, router_rows], axis=1), "seq", 0, 0, tiled=True
        )
    partial_size = partial.shape[1]
    parts = received[:, :partial_size].reshape(seq_size, head_groups, new_count, head_extent + 2)
    router_full = (
        received[:, partial_size:].reshape(seq_size * part_width, -1).astype(jnp.bfloat16)
    )

    with jax.named_scope("merge_request"):
        own_queries = lax.dynamic_index_in_dim(queries, own_request, 0, keepdims=False)[:, 0]
        own_keys = lax.dynamic_index_in_dim(new_keys, own_request, 0, keepdims=False)[:, 0]
        own_values = lax.dynamic_index_in_dim(new_values, own_request, 0, keepdims=False)[:, 0]
        new_scores = (
            jnp.einsum("tqe,se->qts", own_queries, own_keys, preferred_element_type=jnp.float32)
            * SCORE_SCALE
        )
        newest = jnp.arange(new_count, dtype=jnp.int32)
        causal = newest[None, :] <= newest[:, None]
        new_masked = jnp.where(causal, new_scores, NEG_LARGE)
        new_top = jnp.max(new_masked, axis=-1)
        new_probs = jnp.where(causal, jnp.exp(new_masked - new_top[..., None]), 0.0)
        new_sums = jnp.einsum(
            "qts,se->qte",
            new_probs.astype(jnp.bfloat16),
            own_values,
            preferred_element_type=jnp.float32,
        )
        part_sums = parts[..., :head_extent]
        part_totals = parts[..., head_extent]
        part_tops = parts[..., head_extent + 1]
        highest = jnp.maximum(jnp.max(part_tops, axis=0), new_top)
        part_scale = jnp.exp(part_tops - highest)
        new_scale = jnp.exp(new_top - highest)
        joined_totals = jnp.sum(part_totals * part_scale, axis=0) + jnp.sum(new_probs, axis=-1) * new_scale
        joined_sums = (
            jnp.sum(part_sums * part_scale[..., None], axis=0) + new_sums * new_scale[..., None]
        )
        attended = (joined_sums / joined_totals[..., None]).astype(jnp.bfloat16)
        attended = jnp.transpose(attended, (1, 0, 2)).reshape(new_count, head_groups * head_extent)
    attn_part = jnp.dot(attended, output_weight[0], preferred_element_type=jnp.float32)
    with jax.named_scope("sum_heads"):
        attn_rows = butterfly_sum(attn_part, "tp")

    own_inputs = lax.dynamic_index_in_dim(inputs, own_request, 0, keepdims=False)
    whole_rows = own_inputs + attn_rows
    row_scale = lax.rsqrt(jnp.mean(whole_rows * whole_rows, axis=-1, keepdims=True) + EPSILON)
    own_mixed = (whole_rows * row_scale * moe_gain).astype(jnp.bfloat16)
    own_logits = jnp.dot(own_mixed, router_full, preferred_element_type=jnp.float32)

    def by_column_block(values):
        return jnp.transpose(values.reshape(new_count, seq_size, part_width), (1, 0, 2))

    expert_count = own_logits.shape[1]
    outgoing = jnp.concatenate(
        [
            by_column_block(own_mixed.astype(jnp.float32)),
            by_column_block(whole_rows),
            jnp.broadcast_to(own_logits[None], (seq_size, new_count, expert_count)),
        ],
        axis=-1,
    )
    with jax.named_scope("spread_rows"):
        incoming = lax.all_to_all(outgoing, "seq", 0, 0, tiled=True)
    mixed_rows = incoming[..., :part_width].reshape(token_count, part_width).astype(jnp.bfloat16)
    residual = incoming[..., part_width : 2 * part_width].reshape(token_count, part_width)
    logits = incoming[..., 2 * part_width :].reshape(token_count, expert_count)

    experts_here = w_gate_up.shape[0]
    top_count = routes.shape[1]
    capacity = token_count // 2
    pair_count = token_count * top_count
    flat_routes = routes.reshape(-1)
    local_ids = tp_index * experts_here + jnp.arange(experts_here, dtype=jnp.int32)
    onehot = (flat_routes[:, None] == local_ids[None, :]).astype(jnp.bfloat16)
    pair_ids = jnp.arange(pair_count, dtype=jnp.int32)
    earlier = (pair_ids[None, :] < pair_ids[:, None]).astype(jnp.bfloat16)
    before = jnp.dot(earlier, onehot, preferred_element_type=jnp.float32)
    slots = jnp.sum(before * onehot.astype(jnp.float32), axis=1).astype(jnp.int32)
    slots = slots.reshape(token_count, top_count)
    picked = jnp.take_along_axis(logits, routes, axis=1)
    combine = jax.nn.softmax(picked, axis=-1)
    slot_ids = jnp.arange(capacity, dtype=jnp.int32)
    hits = (routes[None, None] == local_ids[:, None, None, None]) & (
        slots[None, None] == slot_ids[None, :, None, None]
    )
    dispatch = jnp.any(hits, axis=-1)
    slot_weight = jnp.sum(jnp.where(hits, combine[None, None], 0.0), axis=(2, 3))

    expert_in = jnp.einsum(
        "ecn,nd->ecd", dispatch.astype(jnp.bfloat16), mixed_rows, preferred_element_type=jnp.float32
    ).astype(jnp.bfloat16)
    both_part = jnp.einsum(
        "ecd,edgh->ecgh", expert_in, w_gate_up, preferred_element_type=jnp.float32
    )
    slot_total = experts_here * capacity
    slots_each = slot_total // seq_size
    both_part = both_part.reshape(seq_size, -1)
    with jax.named_scope("reduce_gate_up"):
        both_pieces = lax.all_to_all(both_part, "seq", 0, 0, tiled=True)
    both = jnp.sum(both_pieces, axis=0).reshape(slots_each, 2, -1)
    own_weight = lax.dynamic_slice_in_dim(
        slot_weight.reshape(-1), seq_index * slots_each, slots_each, 0
    )
    hidden = (jax.nn.silu(both[:, 0]) * both[:, 1] * own_weight[:, None]).astype(jnp.bfloat16)
    hid_width = hidden.shape[1]
    with jax.named_scope("gather_hidden"):
        hidden_all = lax.all_to_all(
            jnp.broadcast_to(hidden[None], (seq_size, slots_each, hid_width)),
            "seq",
            0,
            0,
            tiled=True,
        )
    hidden_all = hidden_all.reshape(experts_here, capacity, hid_width)
    expert_out = jnp.einsum(
        "ech,edh->ecd", hidden_all, w_down, preferred_element_type=jnp.float32
    )
    moe_part = jnp.einsum(
        "ecn,ecd->nd", dispatch.astype(jnp.float32), expert_out, precision=lax.Precision.HIGHEST
    )
    row_count = token_count // tp_size
    with jax.named_scope("reduce_experts"):
        moe_pieces = lax.all_to_all(
            moe_part.reshape(tp_size, row_count, part_width), "tp", 0, 0, tiled=True
        )
    moe_rows = jnp.sum(moe_pieces, axis=0)
    base_rows = lax.dynamic_slice_in_dim(residual, tp_index * row_count, row_count, 0)
    return (base_rows + moe_rows).astype(jnp.bfloat16)


def solution(mesh):
    in_specs = (
        P(),
        P(),
        P(),
        P(),
        P(None, "tp", None),
        P(None, "tp", "seq", None),
        P(None, "tp", "seq", None),
        P("tp", None, None),
        P(),
        P("seq", None),
        P("tp", "seq", None, None),
        P("tp", "seq", None),
    )
    out_specs = P("tp", "seq")
    return jax.shard_map(
        per_device, mesh=mesh, in_specs=in_specs, out_specs=out_specs, check_vma=False
    )
```

```python
import jax
import jax.numpy as jnp
from jax import lax
from jax.sharding import PartitionSpec as P

EPSILON = 1e-06
ROPE_BASE = 10000.0
SCORE_SCALE = 0.125
NEG_LARGE = -1e30


def rotate(values, angles):
    half = values.shape[-1] // 2
    cosine = jnp.cos(angles)
    sine = jnp.sin(angles)
    front = values[..., :half]
    back = values[..., half:]
    return jnp.concatenate([front * cosine - back * sine, back * cosine + front * sine], axis=-1)


def butterfly_sum(values, axis):
    count = lax.axis_size(axis)
    step = 1
    while step < count:
        pairs = [(i, i ^ step) for i in range(count)]
        values = values + lax.ppermute(values, axis, pairs)
        step *= 2
    return values


def per_device(
    embedded,
    lengths,
    routes,
    attn_gain,
    query_key_value_weight,
    cache_k,
    value_cache,
    output_weight,
    moe_gain,
    w_router,
    w_gate_up,
    w_down,
):
    requests, new_count, width = embedded.shape
    token_count = requests * new_count
    head_extent = cache_k.shape[3]
    head_groups = query_key_value_weight.shape[2] // head_extent - 2
    ctx_here = cache_k.shape[2]
    part_width = w_router.shape[0]
    seq_size = lax.axis_size("seq")
    tp_size = lax.axis_size("tp")
    seq_index = lax.axis_index("seq")
    tp_index = lax.axis_index("tp")
    own_request = seq_index * (requests // seq_size)

    with jax.named_scope("gather_router"):
        router_full = lax.all_to_all(
            jnp.broadcast_to(w_router[None], (seq_size,) + w_router.shape), "seq", 0, 0, tiled=True
        ).reshape(seq_size * part_width, -1)

    inputs = embedded.astype(jnp.float32)
    stat = jnp.mean(inputs * inputs, axis=-1, keepdims=True)
    normed = (inputs * lax.rsqrt(stat + EPSILON) * attn_gain).astype(jnp.bfloat16)
    projected_rows = jnp.einsum(
        "rtd,dhc->rthc", normed, query_key_value_weight, preferred_element_type=jnp.float32
    )
    split_parts = projected_rows.reshape(requests, new_count, 1, head_groups + 2, head_extent)
    half = head_extent // 2
    freqs = ROPE_BASE ** (-jnp.arange(half, dtype=jnp.float32) / half)
    positions = (
        lengths.astype(jnp.float32)[:, None] + jnp.arange(new_count, dtype=jnp.float32)[None, :]
    )
    angles = positions[:, :, None] * freqs
    queries = rotate(split_parts[:, :, :, :head_groups], angles[:, :, None, None, :]).astype(
        jnp.bfloat16
    )
    new_keys = rotate(split_parts[:, :, :, head_groups], angles[:, :, None, :]).astype(jnp.bfloat16)
    new_values = split_parts[:, :, :, head_groups + 1].astype(jnp.bfloat16)

    with jax.named_scope("cache_attention"):
        scores = (
            jnp.einsum("rthqe,rhpe->rhqtp", queries, cache_k, preferred_element_type=jnp.float32)
            * SCORE_SCALE
        )
        places = seq_index * ctx_here + jnp.arange(ctx_here, dtype=jnp.int32)
        live = (places[None, :] < lengths[:, None])[:, None, None, None, :]
        masked = jnp.where(live, scores, NEG_LARGE)
        local_top = jnp.max(masked, axis=-1)
        probs = jnp.where(live, jnp.exp(masked - local_top[..., None]), 0.0)
        totals = jnp.sum(probs, axis=-1)
        sums = jnp.einsum(
            "rhqtp,rhpe->rhqte",
            probs.astype(jnp.bfloat16),
            value_cache,
            preferred_element_type=jnp.float32,
        )
    partial = jnp.concatenate([sums, totals[..., None], local_top[..., None]], axis=-1)
    partial = partial.reshape(seq_size, head_groups, new_count, head_extent + 2)
    with jax.named_scope("gather_partials"):
        parts = lax.all_to_all(partial, "seq", 0, 0, tiled=True)

    with jax.named_scope("merge_request"):
        own_queries = lax.dynamic_index_in_dim(queries, own_request, 0, keepdims=False)[:, 0]
        own_keys = lax.dynamic_index_in_dim(new_keys, own_request, 0, keepdims=False)[:, 0]
        own_values = lax.dynamic_index_in_dim(new_values, own_request, 0, keepdims=False)[:, 0]
        new_scores = (
            jnp.einsum("tqe,se->qts", own_queries, own_keys, preferred_element_type=jnp.float32)
            * SCORE_SCALE
        )
        newest = jnp.arange(new_count, dtype=jnp.int32)
        causal = newest[None, :] <= newest[:, None]
        new_masked = jnp.where(causal, new_scores, NEG_LARGE)
        new_top = jnp.max(new_masked, axis=-1)
        new_probs = jnp.where(causal, jnp.exp(new_masked - new_top[..., None]), 0.0)
        new_sums = jnp.einsum(
            "qts,se->qte",
            new_probs.astype(jnp.bfloat16),
            own_values,
            preferred_element_type=jnp.float32,
        )
        part_sums = parts[..., :head_extent]
        part_totals = parts[..., head_extent]
        part_tops = parts[..., head_extent + 1]
        highest = jnp.maximum(jnp.max(part_tops, axis=0), new_top)
        part_scale = jnp.exp(part_tops - highest)
        new_scale = jnp.exp(new_top - highest)
        joined_totals = jnp.sum(part_totals * part_scale, axis=0) + jnp.sum(new_probs, axis=-1) * new_scale
        joined_sums = (
            jnp.sum(part_sums * part_scale[..., None], axis=0) + new_sums * new_scale[..., None]
        )
        attended = (joined_sums / joined_totals[..., None]).astype(jnp.bfloat16)
        attended = jnp.transpose(attended, (1, 0, 2)).reshape(new_count, head_groups * head_extent)
    attn_part = jnp.dot(attended, output_weight[0], preferred_element_type=jnp.float32)
    with jax.named_scope("sum_heads"):
        attn_rows = butterfly_sum(attn_part, "tp")

    own_inputs = lax.dynamic_index_in_dim(inputs, own_request, 0, keepdims=False)
    whole_rows = own_inputs + attn_rows
    row_scale = lax.rsqrt(jnp.mean(whole_rows * whole_rows, axis=-1, keepdims=True) + EPSILON)
    own_mixed = (whole_rows * row_scale * moe_gain).astype(jnp.bfloat16)
    own_logits = jnp.dot(own_mixed, router_full, preferred_element_type=jnp.float32)

    def by_column_block(values):
        return jnp.transpose(values.reshape(new_count, seq_size, part_width), (1, 0, 2))

    expert_count = own_logits.shape[1]
    outgoing = jnp.concatenate(
        [
            by_column_block(own_mixed.astype(jnp.float32)),
            by_column_block(whole_rows),
            jnp.broadcast_to(own_logits[None], (seq_size, new_count, expert_count)),
        ],
        axis=-1,
    )
    with jax.named_scope("spread_rows"):
        incoming = lax.all_to_all(outgoing, "seq", 0, 0, tiled=True)
    mixed_rows = incoming[..., :part_width].reshape(token_count, part_width).astype(jnp.bfloat16)
    residual = incoming[..., part_width : 2 * part_width].reshape(token_count, part_width)
    logits = incoming[..., 2 * part_width :].reshape(token_count, expert_count)

    experts_here = w_gate_up.shape[0]
    top_count = routes.shape[1]
    capacity = token_count // 2
    pair_count = token_count * top_count
    flat_routes = routes.reshape(-1)
    local_ids = tp_index * experts_here + jnp.arange(experts_here, dtype=jnp.int32)
    onehot = (flat_routes[:, None] == local_ids[None, :]).astype(jnp.bfloat16)
    pair_ids = jnp.arange(pair_count, dtype=jnp.int32)
    earlier = (pair_ids[None, :] < pair_ids[:, None]).astype(jnp.bfloat16)
    before = jnp.dot(earlier, onehot, preferred_element_type=jnp.float32)
    slots = jnp.sum(before * onehot.astype(jnp.float32), axis=1).astype(jnp.int32)
    slots = slots.reshape(token_count, top_count)
    choose = routes[:, :, None] == jnp.arange(expert_count, dtype=jnp.int32)[None, None, :]
    picked = jnp.sum(jnp.where(choose, logits[:, None, :], 0.0), axis=-1)
    combine = jax.nn.softmax(picked, axis=-1)
    slot_ids = jnp.arange(capacity, dtype=jnp.int32)
    hits = (routes[None, None] == local_ids[:, None, None, None]) & (
        slots[None, None] == slot_ids[None, :, None, None]
    )
    dispatch = jnp.any(hits, axis=-1)
    slot_weight = jnp.sum(jnp.where(hits, combine[None, None], 0.0), axis=(2, 3))

    expert_in = jnp.einsum(
        "ecn,nd->ecd", dispatch.astype(jnp.bfloat16), mixed_rows, preferred_element_type=jnp.float32
    ).astype(jnp.bfloat16)
    both_part = jnp.einsum(
        "ecd,edgh->ecgh", expert_in, w_gate_up, preferred_element_type=jnp.float32
    )
    slot_total = experts_here * capacity
    slots_each = slot_total // seq_size
    both_part = both_part.astype(jnp.bfloat16).reshape(seq_size, slots_each, -1)
    with jax.named_scope("reduce_gate_up"):
        both_pieces = lax.all_to_all(both_part, "seq", 0, 0, tiled=True)
    both = jnp.sum(both_pieces.astype(jnp.float32), axis=0).reshape(slots_each, 2, -1)
    own_weight = lax.dynamic_slice_in_dim(
        slot_weight.reshape(-1), seq_index * slots_each, slots_each, 0
    )
    hidden = (jax.nn.silu(both[:, 0]) * both[:, 1] * own_weight[:, None]).astype(jnp.bfloat16)
    hid_width = hidden.shape[1]
    with jax.named_scope("gather_hidden"):
        hidden_all = lax.all_to_all(
            jnp.broadcast_to(hidden[None], (seq_size, slots_each, hid_width)),
            "seq",
            0,
            0,
            tiled=True,
        )
    hidden_all = hidden_all.reshape(experts_here, capacity, hid_width)
    expert_out = jnp.einsum(
        "ech,edh->ecd", hidden_all, w_down, preferred_element_type=jnp.float32
    )
    moe_part = jnp.einsum(
        "ecn,ecd->nd", dispatch.astype(jnp.float32), expert_out, precision=lax.Precision.HIGHEST
    )
    row_count = token_count // tp_size
    with jax.named_scope("reduce_experts"):
        moe_pieces = lax.all_to_all(
            moe_part.reshape(tp_size, row_count, part_width), "tp", 0, 0, tiled=True
        )
    moe_rows = jnp.sum(moe_pieces, axis=0)
    base_rows = lax.dynamic_slice_in_dim(residual, tp_index * row_count, row_count, 0)
    return (base_rows + moe_rows).astype(jnp.bfloat16)


def solution(mesh):
    in_specs = (
        P(),
        P(),
        P(),
        P(),
        P(None, "tp", None),
        P(None, "tp", "seq", None),
        P(None, "tp", "seq", None),
        P("tp", None, None),
        P(),
        P("seq", None),
        P("tp", "seq", None, None),
        P("tp", "seq", None),
    )
    out_specs = P("tp", "seq")
    return jax.shard_map(
        per_device, mesh=mesh, in_specs=in_specs, out_specs=out_specs, check_vma=False
    )
```
